512 devices in a mesh: strip: 512 (over z, y, x, core).
Axes of the slice: x: 4, y: 4, z: 16, core: 2. Of those that a mesh axis runs over, the one named last changes fastest.
Arguments:
- velocity: float32 [2, 128, 2048, 768], P(None, None, 'strip'), may hold values from -100 to 100
Outputs:
- spatial_modes: float32 [128, 2048, 768], P(None, 'strip')
- triangle: float32 [128, 128], replicated
The draws below stay inside these ranges and needn't reach their ends.
All inputs are finite; a program needn't handle non-finite values.
Results may differ from the reference program's by a relative error of at most 0.000094.
Values sent between devices are 32-bit elements; how exact they have to be, the bound alone decides.
No kernel may reach another device: no remote copies, remote signals or barrier semaphores. Data moves between devices by JAX's collectives and lax.ppermute only.
A program may use at most 128 MiB of HBM per device.

```python
import math
import jax
import jax.numpy as jnp
from jax import lax

K = 128
NY = 768
NX = 2048


def draw_velocity(key, part):
    keys = jax.random.split(key, 4)
    snap_scale = jnp.exp(jax.random.uniform(keys[0], (1, K, 1, 1), jnp.float32, math.log(0.5), math.log(5.0)))
    row_scale = jnp.exp(jax.random.uniform(keys[1], (1, 1, NX, 1), jnp.float32, math.log(0.5), math.log(1.6)))
    col_scale = jnp.exp(jax.random.uniform(keys[2], (1, 1, 1, NY), jnp.float32, math.log(0.5), math.log(1.6)))
    noise = jnp.clip(jax.random.normal(keys[3], (2, K, NX, NY), jnp.float32), -6.0, 6.0)
    return (noise * snap_scale * row_scale * col_scale).astype(jnp.float32)


def setup_inputs(seed: int = 0) -> dict:
    arg_keys = jax.random.split(jax.random.key(seed), 2)
    return {
        "velocity": draw_velocity(jax.random.fold_in(arg_keys[1], 71), 0),
    }


def along_first(field):
    return (8.0 * (jnp.roll(field, -1, 0) - jnp.roll(field, 1, 0)) - (jnp.roll(field, -2, 0) - jnp.roll(field, 2, 0))) / 12.0

def along_second(field):
    return (8.0 * (jnp.roll(field, -1, 1) - jnp.roll(field, 1, 1)) - (jnp.roll(field, -2, 1) - jnp.roll(field, 2, 1))) / 12.0

def reference(velocity):
    zero_index = jnp.zeros((), jnp.int32)
    one_index = jnp.ones((), jnp.int32)

    def one_snapshot(snap_index):
        comp_u = lax.dynamic_slice(velocity, (zero_index, snap_index, zero_index, zero_index), (1, 1, NX, NY))[0, 0]
        comp_v = lax.dynamic_slice(velocity, (one_index, snap_index, zero_index, zero_index), (1, 1, NX, NY))[0, 0]
        return along_first(comp_v) - along_second(comp_u)
    vorticity = lax.map(one_snapshot, jnp.arange(K, dtype=jnp.int32))
    flattened = vorticity.reshape(K, NX * NY)
    gram = jnp.dot(flattened.astype(jnp.float32), flattened.T.astype(jnp.float32), precision=lax.Precision.HIGHEST, preferred_element_type=jnp.float32) / (NX * NY)
    lower = jnp.linalg.cholesky(gram)
    spatial_modes = lax.linalg.triangular_solve(lower, flattened, left_side=True, lower=True)
    return (spatial_modes.reshape(K, NX, NY), lower.T)
```

```python
import jax
import jax.numpy as jnp
from jax import lax
from jax.sharding import PartitionSpec as P


def extended(array, sides, width):
    for axis, dim in sides:
        size, length = (lax.axis_size(axis), array.shape[dim])
        up = [(i, (i + 1) % size) for i in range(size)]
        down = [(j, i) for i, j in up]
        last = lax.slice_in_dim(array, length - width, length, axis=dim)
        initial = lax.slice_in_dim(array, 0, width, axis=dim)
        before = lax.ppermute(last, axis, up)
        after = lax.ppermute(initial, axis, down)
        array = jnp.concatenate([before, array, after], axis=dim)
    return array


def butterfly_sum(value, axis):
    size = lax.axis_size(axis)
    bit = 1
    while bit < size:
        pairs = [(i, i ^ bit) for i in range(size)]
        value = value + lax.ppermute(value, axis, pairs)
        bit *= 2
    return value


def along_second(field):
    return (
        8.0 * (jnp.roll(field, -1, 2) - jnp.roll(field, 1, 2))
        - (jnp.roll(field, -2, 2) - jnp.roll(field, 2, 2))
    ) / 12.0


def stencil_rows(padded, row_count):
    return 8.0 * (padded[:, 3 : row_count + 3] - padded[:, 1 : row_count + 1]) - (
        padded[:, 4 : row_count + 4] - padded[:, 0:row_count]
    )


def local(velocity):
    snap_count = velocity.shape[1]
    row_count = velocity.shape[2]
    col_count = velocity.shape[3]
    total_cells = row_count * lax.axis_size("strip") * col_count
    comp_u = velocity[0]
    comp_v = velocity[1]
    padded = extended(comp_v, (("strip", 1),), 2)
    v_first = stencil_rows(padded, row_count) / 12.0
    vorticity = v_first - along_second(comp_u)
    flattened = vorticity.reshape(snap_count, row_count * col_count)
    local_gram = (
        jnp.dot(
            flattened,
            flattened.T,
            precision=lax.Precision.HIGHEST,
            preferred_element_type=jnp.float32,
        )
        / total_cells
    )
    gram = butterfly_sum(local_gram, "strip")
    lower = jnp.linalg.cholesky(gram)
    identity = jnp.eye(snap_count, dtype=jnp.float32)
    inverse_lower = lax.linalg.triangular_solve(lower, identity, left_side=True, lower=True)
    spatial_modes = jnp.dot(
        inverse_lower,
        flattened,
        precision=lax.Precision.HIGHEST,
        preferred_element_type=jnp.float32,
    )
    return (spatial_modes.reshape(snap_count, row_count, col_count), lower.T)


def solution(mesh):
    return jax.shard_map(
        local,
        mesh=mesh,
        in_specs=(P(None, None, "strip", None),),
        out_specs=(P(None, "strip", None), P()),
        check_vma=False,
    )
```

```python
import jax
import jax.numpy as jnp
from jax import lax
from jax.sharding import Mesh
from jax.sharding import PartitionSpec as P

AXES = ("zh", "zl", "y", "x", "core")


def ring_index(shape):
    size = 1
    for s in shape:
        size *= s
    return size


def extended(array, axes, size, dim, width):
    length = array.shape[dim]
    up = [(i, (i + 1) % size) for i in range(size)]
    down = [(j, i) for i, j in up]
    last = lax.slice_in_dim(array, length - width, length, axis=dim)
    initial = lax.slice_in_dim(array, 0, width, axis=dim)
    before = lax.ppermute(last, axes, up)
    after = lax.ppermute(initial, axes, down)
    return jnp.concatenate([before, array, after], axis=dim)


def tree_sum(values):
    while len(values) > 1:
        values = [values[i] + values[i + 1] for i in range(0, len(values), 2)]
    return values[0]


def gather_sum(value, axes, count):
    stacked = jnp.broadcast_to(value[None], (count,) + value.shape)
    gathered = lax.all_to_all(stacked, axes, 0, 0, tiled=True)
    return tree_sum([gathered[m] for m in range(count)])


def butterfly_sum(value, axis, size):
    bit = 1
    while bit < size:
        pairs = [(i, i ^ bit) for i in range(size)]
        value = value + lax.ppermute(value, axis, pairs)
        bit *= 2
    return value


def along_second(field):
    return (
        8.0 * (jnp.roll(field, -1, 2) - jnp.roll(field, 1, 2))
        - (jnp.roll(field, -2, 2) - jnp.roll(field, 2, 2))
    ) / 12.0


def stencil_rows(padded, row_count):
    return 8.0 * (padded[:, 3 : row_count + 3] - padded[:, 1 : row_count + 1]) - (
        padded[:, 4 : row_count + 4] - padded[:, 0:row_count]
    )


def make_local(sizes):
    total = ring_index(sizes.values())

    def local(velocity):
        snap_count = velocity.shape[1]
        row_count = velocity.shape[2]
        col_count = velocity.shape[3]
        total_cells = row_count * total * col_count
        comp_u = velocity[0]
        comp_v = velocity[1]
        padded = extended(comp_v, AXES, total, 1, 2)
        v_first = stencil_rows(padded, row_count) / 12.0
        vorticity = v_first - along_second(comp_u)
        flattened = vorticity.reshape(snap_count, row_count * col_count)
        local_gram = (
            jnp.dot(
                flattened,
                flattened.T,
                precision=lax.Precision.HIGHEST,
                preferred_element_type=jnp.float32,
            )
            / total_cells
        )
        gram = gather_sum(local_gram, ("x", "core"), sizes["x"] * sizes["core"])
        gram = gather_sum(gram, ("y",), sizes["y"])
        gram = gather_sum(gram, ("zl",), sizes["zl"])
        gram = butterfly_sum(gram, "zh", sizes["zh"])
        lower = jnp.linalg.cholesky(gram)
        identity = jnp.eye(snap_count, dtype=jnp.float32)
        inverse_lower = lax.linalg.triangular_solve(lower, identity, left_side=True, lower=True)
        spatial_modes = jnp.dot(
            inverse_lower,
            flattened,
            precision=lax.Precision.HIGHEST,
            preferred_element_type=jnp.float32,
        )
        return (spatial_modes.reshape(snap_count, row_count, col_count), lower.T)

    return local


def solution(mesh):
    devices = mesh.devices.reshape(-1)
    count = devices.shape[0]
    core = 2
    x_size = 4 if count % (core * 4) == 0 else 1
    y_size = 4 if count % (core * x_size * 4) == 0 else 1
    rest = count // (core * x_size * y_size)
    zl = 4 if rest % 4 == 0 else rest
    zh = rest // zl
    sizes = {"zh": zh, "zl": zl, "y": y_size, "x": x_size, "core": core}
    view = Mesh(devices.reshape(zh, zl, y_size, x_size, core), AXES)
    return jax.shard_map(
        make_local(sizes),
        mesh=view,
        in_specs=(P(None, None, AXES, None),),
        out_specs=(P(None, AXES, None), P()),
        check_vma=False,
    )
```

```python
import jax
import jax.numpy as jnp
from jax import lax
from jax.experimental import pallas as pl
from jax.experimental.pallas import tpu as pltpu
from jax.sharding import Mesh
from jax.sharding import PartitionSpec as P

AXES = ("zh", "zl", "y", "x", "core")


def ring_index(shape):
    size = 1
    for s in shape:
        size *= s
    return size


def extended(array, axes, size, dim, width):
    length = array.shape[dim]
    up = [(i, (i + 1) % size) for i in range(size)]
    down = [(j, i) for i, j in up]
    last = lax.slice_in_dim(array, length - width, length, axis=dim)
    initial = lax.slice_in_dim(array, 0, width, axis=dim)
    before = lax.ppermute(last, axes, up)
    after = lax.ppermute(initial, axes, down)
    return jnp.concatenate([before, array, after], axis=dim)


def factor_kernel(gram_ref, upper_ref, inverse_ref, rest_ref, ops_ref):
    size = gram_ref.shape[0]
    rows = lax.broadcasted_iota(jnp.int32, (size, size), 0)
    cols = lax.broadcasted_iota(jnp.int32, (size, size), 1)
    lane = lax.broadcasted_iota(jnp.int32, (1, size), 1)
    sublane = lax.broadcasted_iota(jnp.int32, (size, 1), 0)
    rest_ref[...] = gram_ref[...]
    ops_ref[...] = jnp.where(rows == cols, 1.0, 0.0).astype(jnp.float32)

    def step(j, carry):
        rest = rest_ref[...]
        row = rest_ref[pl.ds(j, 1), :]
        ops_row = ops_ref[pl.ds(j, 1), :]
        pivot = jnp.sum(jnp.where(lane == j, row, 0.0), axis=1, keepdims=True)
        root = jnp.sqrt(pivot)
        factor_row = jnp.where(lane >= j, row / root, 0.0)
        inverse_row = ops_row / root
        upper_ref[pl.ds(j, 1), :] = factor_row
        inverse_ref[pl.ds(j, 1), :] = inverse_row
        column = jnp.sum(jnp.where(cols == j, rest, 0.0), axis=1, keepdims=True)
        factor_col = jnp.where(sublane > j, column / root, 0.0)
        rest_ref[...] = rest - factor_col * factor_row
        ops_ref[...] = ops_ref[...] - factor_col * inverse_row
        return carry

    lax.fori_loop(0, size, step, 0)


def factor(gram):
    size = gram.shape[0]
    vmem = pltpu.VMEM
    return pl.pallas_call(
        factor_kernel,
        out_shape=(
            jax.ShapeDtypeStruct((size, size), jnp.float32),
            jax.ShapeDtypeStruct((size, size), jnp.float32),
        ),
        in_specs=[pl.BlockSpec(memory_space=vmem)],
        out_specs=(pl.BlockSpec(memory_space=vmem), pl.BlockSpec(memory_space=vmem)),
        scratch_shapes=[vmem((size, size), jnp.float32), vmem((size, size), jnp.float32)],
    )(gram)


def tree_sum(values):
    while len(values) > 1:
        values = [values[i] + values[i + 1] for i in range(0, len(values), 2)]
    return values[0]


def gather_sum(value, axes, count):
    stacked = jnp.broadcast_to(value[None], (count,) + value.shape)
    gathered = lax.all_to_all(stacked, axes, 0, 0, tiled=True)
    return tree_sum([gathered[m] for m in range(count)])


def butterfly_sum(value, axis, size):
    bit = 1
    while bit < size:
        pairs = [(i, i ^ bit) for i in range(size)]
        value = value + lax.ppermute(value, axis, pairs)
        bit *= 2
    return value


def along_second(field):
    return (
        8.0 * (jnp.roll(field, -1, 2) - jnp.roll(field, 1, 2))
        - (jnp.roll(field, -2, 2) - jnp.roll(field, 2, 2))
    ) / 12.0


def stencil_rows(padded, row_count):
    return 8.0 * (padded[:, 3 : row_count + 3] - padded[:, 1 : row_count + 1]) - (
        padded[:, 4 : row_count + 4] - padded[:, 0:row_count]
    )


def make_local(sizes):
    total = ring_index(sizes.values())

    def local(velocity):
        snap_count = velocity.shape[1]
        row_count = velocity.shape[2]
        col_count = velocity.shape[3]
        total_cells = row_count * total * col_count
        comp_u = velocity[0]
        comp_v = velocity[1]
        padded = extended(comp_v, AXES, total, 1, 2)
        v_first = stencil_rows(padded, row_count) / 12.0
        vorticity = v_first - along_second(comp_u)
        flattened = vorticity.reshape(snap_count, row_count * col_count)
        local_gram = (
            jnp.dot(
                flattened,
                flattened.T,
                precision=lax.Precision.HIGHEST,
                preferred_element_type=jnp.float32,
            )
            / total_cells
        )
        gram = gather_sum(local_gram, ("x", "core"), sizes["x"] * sizes["core"])
        gram = gather_sum(gram, ("y",), sizes["y"])
        gram = gather_sum(gram, ("zl",), sizes["zl"])
        gram = butterfly_sum(gram, "zh", sizes["zh"])
        upper, inverse_lower = factor(gram)
        spatial_modes = jnp.dot(
            inverse_lower,
            flattened,
            precision=lax.Precision.HIGHEST,
            preferred_element_type=jnp.float32,
        )
        return (spatial_modes.reshape(snap_count, row_count, col_count), upper)

    return local


def solution(mesh):
    devices = mesh.devices.reshape(-1)
    count = devices.shape[0]
    core = 2
    x_size = 4 if count % (core * 4) == 0 else 1
    y_size = 4 if count % (core * x_size * 4) == 0 else 1
    rest = count // (core * x_size * y_size)
    zl = 4 if rest % 4 == 0 else rest
    zh = rest // zl
    sizes = {"zh": zh, "zl": zl, "y": y_size, "x": x_size, "core": core}
    view = Mesh(devices.reshape(zh, zl, y_size, x_size, core), AXES)
    return jax.shard_map(
        make_local(sizes),
        mesh=view,
        in_specs=(P(None, None, AXES, None),),
        out_specs=(P(None, AXES, None), P()),
        check_vma=False,
    )
```

```python
import jax
import jax.numpy as jnp
from jax import lax
from jax.experimental import pallas as pl
from jax.experimental.pallas import tpu as pltpu
from jax.sharding import Mesh
from jax.sharding import PartitionSpec as P

AXES = ("zh", "zl", "y", "x", "core")


def ring_index(shape):
    size = 1
    for s in shape:
        size *= s
    return size


def extended(array, axes, size, dim, width):
    length = array.shape[dim]
    up = [(i, (i + 1) % size) for i in range(size)]
    down = [(j, i) for i, j in up]
    last = lax.slice_in_dim(array, length - width, length, axis=dim)
    initial = lax.slice_in_dim(array, 0, width, axis=dim)
    before = lax.ppermute(last, axes, up)
    after = lax.ppermute(initial, axes, down)
    return jnp.concatenate([before, array, after], axis=dim)


def factor_kernel(gram_ref, upper_ref, inverse_ref, rest_ref, ops_ref):
    size = gram_ref.shape[0]
    rows = lax.broadcasted_iota(jnp.int32, (size, size), 0)
    cols = lax.broadcasted_iota(jnp.int32, (size, size), 1)
    lane = lax.broadcasted_iota(jnp.int32, (1, size), 1)
    sublane = lax.broadcasted_iota(jnp.int32, (size, 1), 0)
    rest_ref[...] = gram_ref[...]
    ops_ref[...] = jnp.where(rows == cols, 1.0, 0.0).astype(jnp.float32)

    def step(j, carry):
        rest = rest_ref[...]
        row = rest_ref[pl.ds(j, 1), :]
        ops_row = ops_ref[pl.ds(j, 1), :]
        pivot = jnp.sum(jnp.where(lane == j, row, 0.0), axis=1, keepdims=True)
        scale = lax.rsqrt(pivot)
        factor_row = jnp.where(lane >= j, row * scale, 0.0)
        inverse_row = ops_row * scale
        upper_ref[pl.ds(j, 1), :] = factor_row
        inverse_ref[pl.ds(j, 1), :] = inverse_row
        column = jnp.sum(jnp.where(cols == j, rest, 0.0), axis=1, keepdims=True)
        factor_col = jnp.where(sublane > j, column * scale, 0.0)
        rest_ref[...] = rest - factor_col * factor_row
        ops_ref[...] = ops_ref[...] - factor_col * inverse_row
        return carry

    lax.fori_loop(0, size, step, 0, unroll=2)


def factor(gram):
    size = gram.shape[0]
    vmem = pltpu.VMEM
    return pl.pallas_call(
        factor_kernel,
        out_shape=(
            jax.ShapeDtypeStruct((size, size), jnp.float32),
            jax.ShapeDtypeStruct((size, size), jnp.float32),
        ),
        in_specs=[pl.BlockSpec(memory_space=vmem)],
        out_specs=(pl.BlockSpec(memory_space=vmem), pl.BlockSpec(memory_space=vmem)),
        scratch_shapes=[vmem((size, size), jnp.float32), vmem((size, size), jnp.float32)],
    )(gram)


def tree_sum(values):
    while len(values) > 1:
        values = [values[i] + values[i + 1] for i in range(0, len(values), 2)]
    return values[0]


def gather_sum(value, axes, count):
    stacked = jnp.broadcast_to(value[None], (count,) + value.shape)
    gathered = lax.all_to_all(stacked, axes, 0, 0, tiled=True)
    return tree_sum([gathered[m] for m in range(count)])


def butterfly_sum(value, axis, size):
    bit = 1
    while bit < size:
        pairs = [(i, i ^ bit) for i in range(size)]
        value = value + lax.ppermute(value, axis, pairs)
        bit *= 2
    return value


def along_second(field):
    return (
        8.0 * (jnp.roll(field, -1, 2) - jnp.roll(field, 1, 2))
        - (jnp.roll(field, -2, 2) - jnp.roll(field, 2, 2))
    ) / 12.0


def stencil_rows(padded, row_count):
    return 8.0 * (padded[:, 3 : row_count + 3] - padded[:, 1 : row_count + 1]) - (
        padded[:, 4 : row_count + 4] - padded[:, 0:row_count]
    )


def make_local(sizes):
    total = ring_index(sizes.values())

    def local(velocity):
        snap_count = velocity.shape[1]
        row_count = velocity.shape[2]
        col_count = velocity.shape[3]
        total_cells = row_count * total * col_count
        comp_u = velocity[0]
        comp_v = velocity[1]
        padded = extended(comp_v, AXES, total, 1, 2)
        u_second = lax.optimization_barrier(along_second(comp_u))
        v_first = stencil_rows(padded, row_count) / 12.0
        vorticity = v_first - u_second
        flattened = vorticity.reshape(snap_count, row_count * col_count)
        local_gram = (
            jnp.dot(
                flattened,
                flattened.T,
                precision=lax.Precision.HIGHEST,
                preferred_element_type=jnp.float32,
            )
            / total_cells
        )
        gram = gather_sum(local_gram, ("x", "core"), sizes["x"] * sizes["core"])
        gram = gather_sum(gram, ("y",), sizes["y"])
        gram = gather_sum(gram, ("zl",), sizes["zl"])
        gram = butterfly_sum(gram, "zh", sizes["zh"])
        upper, inverse_lower = factor(gram)
        spatial_modes = jnp.dot(
            inverse_lower,
            flattened,
            precision=lax.Precision.HIGHEST,
            preferred_element_type=jnp.float32,
        )
        return (spatial_modes.reshape(snap_count, row_count, col_count), upper)

    return local


def solution(mesh):
    devices = mesh.devices.reshape(-1)
    count = devices.shape[0]
    core = 2
    x_size = 4 if count % (core * 4) == 0 else 1
    y_size = 4 if count % (core * x_size * 4) == 0 else 1
    rest = count // (core * x_size * y_size)
    zl = 4 if rest % 4 == 0 else rest
    zh = rest // zl
    sizes = {"zh": zh, "zl": zl, "y": y_size, "x": x_size, "core": core}
    view = Mesh(devices.reshape(zh, zl, y_size, x_size, core), AXES)
    return jax.shard_map(
        make_local(sizes),
        mesh=view,
        in_specs=(P(None, None, AXES, None),),
        out_specs=(P(None, AXES, None), P()),
        check_vma=False,
    )
```

```python
import jax
import jax.numpy as jnp
from jax import lax
from jax.experimental import pallas as pl
from jax.experimental.pallas import tpu as pltpu
from jax.sharding import Mesh
from jax.sharding import PartitionSpec as P

AXES = ("zh", "zl", "y", "x", "core")


def ring_index(shape):
    size = 1
    for s in shape:
        size *= s
    return size


def extended(array, axes, size, dim, width):
    length = array.shape[dim]
    up = [(i, (i + 1) % size) for i in range(size)]
    down = [(j, i) for i, j in up]
    last = lax.slice_in_dim(array, length - width, length, axis=dim)
    initial = lax.slice_in_dim(array, 0, width, axis=dim)
    before = lax.ppermute(last, axes, up)
    after = lax.ppermute(initial, axes, down)
    return jnp.concatenate([before, array, after], axis=dim)


def factor_kernel(gram_ref, upper_ref, inverse_ref, rest_ref, ops_ref):
    size = gram_ref.shape[0]
    rows = lax.broadcasted_iota(jnp.int32, (size, size), 0)
    cols = lax.broadcasted_iota(jnp.int32, (size, size), 1)
    lane = lax.broadcasted_iota(jnp.int32, (1, size), 1)
    sublane = lax.broadcasted_iota(jnp.int32, (size, 1), 0)
    rest_ref[...] = gram_ref[...]
    ops_ref[...] = jnp.where(rows == cols, 1.0, 0.0).astype(jnp.float32)

    def step(j, carry):
        rest = rest_ref[...]
        row = rest_ref[pl.ds(j, 1), :]
        ops_row = ops_ref[pl.ds(j, 1), :]
        pivot = jnp.sum(jnp.where(lane == j, row, 0.0), axis=1, keepdims=True)
        scale = lax.rsqrt(pivot)
        factor_row = jnp.where(lane >= j, row * scale, 0.0)
        inverse_row = ops_row * scale
        upper_ref[pl.ds(j, 1), :] = factor_row
        inverse_ref[pl.ds(j, 1), :] = inverse_row
        column = jnp.sum(jnp.where(cols == j, rest, 0.0), axis=1, keepdims=True)
        factor_col = jnp.where(sublane > j, column * scale, 0.0)
        rest_ref[...] = rest - factor_col * factor_row
        ops_ref[...] = ops_ref[...] - factor_col * inverse_row
        return carry

    lax.fori_loop(0, size, step, 0, unroll=2)


def factor(gram):
    size = gram.shape[0]
    vmem = pltpu.VMEM
    return pl.pallas_call(
        factor_kernel,
        out_shape=(
            jax.ShapeDtypeStruct((size, size), jnp.float32),
            jax.ShapeDtypeStruct((size, size), jnp.float32),
        ),
        in_specs=[pl.BlockSpec(memory_space=vmem)],
        out_specs=(pl.BlockSpec(memory_space=vmem), pl.BlockSpec(memory_space=vmem)),
        scratch_shapes=[vmem((size, size), jnp.float32), vmem((size, size), jnp.float32)],
    )(gram)


def pack_symmetric(gram):
    half = gram.shape[0] // 2
    rows = lax.broadcasted_iota(jnp.int32, (half, half), 0)
    cols = lax.broadcasted_iota(jnp.int32, (half, half), 1)
    top, corner, bottom = gram[:half, :half], gram[:half, half:], gram[half:, half:]
    folded = jnp.where(rows <= cols, top, bottom)
    diagonal = jnp.sum(jnp.where(rows == cols, bottom, 0.0), axis=0, keepdims=True)
    tail = jnp.concatenate([diagonal, jnp.zeros_like(diagonal)], axis=1)
    return jnp.concatenate([jnp.concatenate([corner, folded], axis=1), tail], axis=0)


def unpack_symmetric(packed):
    half = packed.shape[1] // 2
    rows = lax.broadcasted_iota(jnp.int32, (half, half), 0)
    cols = lax.broadcasted_iota(jnp.int32, (half, half), 1)
    corner, folded = packed[:half, :half], packed[:half, half:]
    diagonal = packed[half : half + 1, :half]
    flipped = folded.T
    top = jnp.where(rows <= cols, folded, flipped)
    bottom = jnp.where(rows > cols, folded, jnp.where(rows < cols, flipped, diagonal))
    upper = jnp.concatenate([top, corner], axis=1)
    lower = jnp.concatenate([corner.T, bottom], axis=1)
    return jnp.concatenate([upper, lower], axis=0)


def tree_sum(values):
    while len(values) > 1:
        values = [values[i] + values[i + 1] for i in range(0, len(values), 2)]
    return values[0]


def gather_sum(value, axes, count):
    stacked = jnp.broadcast_to(value[None], (count,) + value.shape)
    gathered = lax.all_to_all(stacked, axes, 0, 0, tiled=True)
    return tree_sum([gathered[m] for m in range(count)])


def butterfly_sum(value, axis, size):
    bit = 1
    while bit < size:
        pairs = [(i, i ^ bit) for i in range(size)]
        value = value + lax.ppermute(value, axis, pairs)
        bit *= 2
    return value


def along_second(field):
    return (
        8.0 * (jnp.roll(field, -1, 2) - jnp.roll(field, 1, 2))
        - (jnp.roll(field, -2, 2) - jnp.roll(field, 2, 2))
    ) / 12.0


def stencil_rows(padded, row_count):
    return 8.0 * (padded[:, 3 : row_count + 3] - padded[:, 1 : row_count + 1]) - (
        padded[:, 4 : row_count + 4] - padded[:, 0:row_count]
    )


def make_local(sizes):
    total = ring_index(sizes.values())

    def local(velocity):
        snap_count = velocity.shape[1]
        row_count = velocity.shape[2]
        col_count = velocity.shape[3]
        total_cells = row_count * total * col_count
        comp_u = velocity[0]
        comp_v = velocity[1]
        padded = extended(comp_v, AXES, total, 1, 2)
        u_second = lax.optimization_barrier(along_second(comp_u))
        v_first = stencil_rows(padded, row_count) / 12.0
        vorticity = v_first - u_second
        flattened = vorticity.reshape(snap_count, row_count * col_count)
        local_gram = (
            jnp.dot(
                flattened,
                flattened.T,
                precision=lax.Precision.HIGHEST,
                preferred_element_type=jnp.float32,
            )
            / total_cells
        )
        gram = pack_symmetric(local_gram)
        gram = gather_sum(gram, ("x", "core"), sizes["x"] * sizes["core"])
        gram = gather_sum(gram, ("y",), sizes["y"])
        gram = gather_sum(gram, ("zl",), sizes["zl"])
        gram = butterfly_sum(gram, "zh", sizes["zh"])
        gram = unpack_symmetric(gram)
        upper, inverse_lower = factor(gram)
        spatial_modes = jnp.dot(
            inverse_lower,
            flattened,
            precision=lax.Precision.HIGHEST,
            preferred_element_type=jnp.float32,
        )
        return (spatial_modes.reshape(snap_count, row_count, col_count), upper)

    return local


def solution(mesh):
    devices = mesh.devices.reshape(-1)
    count = devices.shape[0]
    core = 2
    x_size = 4 if count % (core * 4) == 0 else 1
    y_size = 4 if count % (core * x_size * 4) == 0 else 1
    rest = count // (core * x_size * y_size)
    zl = 4 if rest % 4 == 0 else rest
    zh = rest // zl
    sizes = {"zh": zh, "zl": zl, "y": y_size, "x": x_size, "core": core}
    view = Mesh(devices.reshape(zh, zl, y_size, x_size, core), AXES)
    return jax.shard_map(
        make_local(sizes),
        mesh=view,
        in_specs=(P(None, None, AXES, None),),
        out_specs=(P(None, AXES, None), P()),
        check_vma=False,
    )
```

```python
import jax
import jax.numpy as jnp
from jax import lax
from jax.experimental import pallas as pl
from jax.experimental.pallas import tpu as pltpu
from jax.sharding import Mesh
from jax.sharding import PartitionSpec as P

AXES = ("zh", "zl", "y", "x", "core")


def ring_index(shape):
    size = 1
    for s in shape:
        size *= s
    return size


def extended(array, axes, size, dim, width):
    length = array.shape[dim]
    up = [(i, (i + 1) % size) for i in range(size)]
    down = [(j, i) for i, j in up]
    last = lax.slice_in_dim(array, length - width, length, axis=dim)
    initial = lax.slice_in_dim(array, 0, width, axis=dim)
    before = lax.ppermute(last, axes, up)
    after = lax.ppermute(initial, axes, down)
    return jnp.concatenate([before, array, after], axis=dim)


def factor_kernel(gram_ref, upper_ref, inverse_ref, rest_ref, ops_ref):
    size = gram_ref.shape[0]
    rows = lax.broadcasted_iota(jnp.int32, (size, size), 0)
    cols = lax.broadcasted_iota(jnp.int32, (size, size), 1)
    lane = lax.broadcasted_iota(jnp.int32, (1, size), 1)
    sublane = lax.broadcasted_iota(jnp.int32, (size, 1), 0)
    rest_ref[...] = gram_ref[...]
    ops_ref[...] = jnp.where(rows == cols, 1.0, 0.0).astype(jnp.float32)

    def step(j, carry):
        rest = rest_ref[...]
        row = rest_ref[pl.ds(j, 1), :]
        ops_row = ops_ref[pl.ds(j, 1), :]
        pivot = jnp.sum(jnp.where(lane == j, row, 0.0), axis=1, keepdims=True)
        scale = lax.rsqrt(pivot)
        factor_row = jnp.where(lane >= j, row * scale, 0.0)
        inverse_row = ops_row * scale
        upper_ref[pl.ds(j, 1), :] = factor_row
        inverse_ref[pl.ds(j, 1), :] = inverse_row
        column = jnp.sum(jnp.where(cols == j, rest, 0.0), axis=1, keepdims=True)
        factor_col = jnp.where(sublane > j, column * scale, 0.0)
        rest_ref[...] = rest - factor_col * factor_row
        ops_ref[...] = ops_ref[...] - factor_col * inverse_row
        return carry

    lax.fori_loop(0, size, step, 0, unroll=2)


def factor(gram):
    size = gram.shape[0]
    vmem = pltpu.VMEM
    return pl.pallas_call(
        factor_kernel,
        out_shape=(
            jax.ShapeDtypeStruct((size, size), jnp.float32),
            jax.ShapeDtypeStruct((size, size), jnp.float32),
        ),
        in_specs=[pl.BlockSpec(memory_space=vmem)],
        out_specs=(pl.BlockSpec(memory_space=vmem), pl.BlockSpec(memory_space=vmem)),
        scratch_shapes=[vmem((size, size), jnp.float32), vmem((size, size), jnp.float32)],
    )(gram)


def pack_symmetric(gram):
    half = gram.shape[0] // 2
    rows = lax.broadcasted_iota(jnp.int32, (half, half), 0)
    cols = lax.broadcasted_iota(jnp.int32, (half, half), 1)
    top, corner, bottom = gram[:half, :half], gram[:half, half:], gram[half:, half:]
    folded = jnp.where(rows <= cols, top, bottom)
    diagonal = jnp.sum(jnp.where(rows == cols, bottom, 0.0), axis=0, keepdims=True)
    tail = jnp.concatenate([diagonal, jnp.zeros_like(diagonal)], axis=1)
    return jnp.concatenate([jnp.concatenate([corner, folded], axis=1), tail], axis=0)


def unpack_symmetric(packed):
    half = packed.shape[1] // 2
    rows = lax.broadcasted_iota(jnp.int32, (half, half), 0)
    cols = lax.broadcasted_iota(jnp.int32, (half, half), 1)
    corner, folded = packed[:half, :half], packed[:half, half:]
    diagonal = packed[half : half + 1, :half]
    flipped = folded.T
    top = jnp.where(rows <= cols, folded, flipped)
    bottom = jnp.where(rows > cols, folded, jnp.where(rows < cols, flipped, diagonal))
    upper = jnp.concatenate([top, corner], axis=1)
    lower = jnp.concatenate([corner.T, bottom], axis=1)
    return jnp.concatenate([upper, lower], axis=0)


def tree_sum(values):
    while len(values) > 1:
        values = [values[i] + values[i + 1] for i in range(0, len(values), 2)]
    return values[0]


def gather_sum(value, axes, count):
    stacked = jnp.broadcast_to(value[None], (count,) + value.shape)
    gathered = lax.all_to_all(stacked, axes, 0, 0, tiled=True)
    return tree_sum([gathered[m] for m in range(count)])


def butterfly_sum(value, axis, size):
    bit = 1
    while bit < size:
        pairs = [(i, i ^ bit) for i in range(size)]
        value = value + lax.ppermute(value, axis, pairs)
        bit *= 2
    return value


def along_second(field):
    return (
        8.0 * (jnp.roll(field, -1, 2) - jnp.roll(field, 1, 2))
        - (jnp.roll(field, -2, 2) - jnp.roll(field, 2, 2))
    ) / 12.0


def stencil_rows(padded, row_count):
    return 8.0 * (padded[:, 3 : row_count + 3] - padded[:, 1 : row_count + 1]) - (
        padded[:, 4 : row_count + 4] - padded[:, 0:row_count]
    )


def make_local(sizes):
    total = ring_index(sizes.values())

    def local(velocity):
        snap_count = velocity.shape[1]
        row_count = velocity.shape[2]
        col_count = velocity.shape[3]
        total_cells = row_count * total * col_count
        comp_u = velocity[0]
        comp_v = velocity[1]
        padded = extended(comp_v, AXES, total, 1, 2)
        u_second = lax.optimization_barrier(along_second(comp_u))
        v_first = stencil_rows(padded, row_count) / 12.0
        vorticity = v_first - u_second
        flattened = vorticity.reshape(snap_count, row_count * col_count)
        local_gram = (
            jnp.dot(
                flattened,
                flattened.T,
                precision=lax.Precision.HIGHEST,
                preferred_element_type=jnp.float32,
            )
            / total_cells
        )
        gram = pack_symmetric(local_gram)
        gram = gather_sum(gram, ("x", "core"), sizes["x"] * sizes["core"])
        gram = gather_sum(gram, ("y",), sizes["y"])
        gram = gather_sum(gram, ("zl",), sizes["zl"])
        gram = gather_sum(gram, ("zh",), sizes["zh"])
        gram = unpack_symmetric(gram)
        upper, inverse_lower = factor(gram)
        spatial_modes = jnp.dot(
            inverse_lower,
            flattened,
            precision=lax.Precision.HIGHEST,
            preferred_element_type=jnp.float32,
        )
        return (spatial_modes.reshape(snap_count, row_count, col_count), upper)

    return local


def solution(mesh):
    devices = mesh.devices.reshape(-1)
    count = devices.shape[0]
    core = 2
    x_size = 4 if count % (core * 4) == 0 else 1
    y_size = 4 if count % (core * x_size * 4) == 0 else 1
    rest = count // (core * x_size * y_size)
    zl = 4 if rest % 4 == 0 else rest
    zh = rest // zl
    sizes = {"zh": zh, "zl": zl, "y": y_size, "x": x_size, "core": core}
    view = Mesh(devices.reshape(zh, zl, y_size, x_size, core), AXES)
    return jax.shard_map(
        make_local(sizes),
        mesh=view,
        in_specs=(P(None, None, AXES, None),),
        out_specs=(P(None, AXES, None), P()),
        check_vma=False,
    )
```

```python
import jax
import jax.numpy as jnp
from jax import lax
from jax.experimental import pallas as pl
from jax.experimental.pallas import tpu as pltpu
from jax.sharding import Mesh
from jax.sharding import PartitionSpec as P

AXES = ("zh", "zl", "y", "x", "core")


def ring_index(shape):
    size = 1
    for s in shape:
        size *= s
    return size


def halo(velocity, axes, size, width):
    length = velocity.shape[2]
    up = [(i, (i + 1) % size) for i in range(size)]
    down = [(j, i) for i, j in up]
    last = velocity[1, :, length - width :, :]
    initial = velocity[1, :, :width, :]
    before = lax.ppermute(last, axes, up)
    after = lax.ppermute(initial, axes, down)
    return before, after


def factor_kernel(gram_ref, upper_ref, inverse_ref, rest_ref, ops_ref):
    size = gram_ref.shape[0]
    rows = lax.broadcasted_iota(jnp.int32, (size, size), 0)
    cols = lax.broadcasted_iota(jnp.int32, (size, size), 1)
    lane = lax.broadcasted_iota(jnp.int32, (1, size), 1)
    sublane = lax.broadcasted_iota(jnp.int32, (size, 1), 0)
    rest_ref[...] = gram_ref[...]
    ops_ref[...] = jnp.where(rows == cols, 1.0, 0.0).astype(jnp.float32)

    def step(j, carry):
        rest = rest_ref[...]
        row = rest_ref[pl.ds(j, 1), :]
        ops_row = ops_ref[pl.ds(j, 1), :]
        pivot = jnp.sum(jnp.where(lane == j, row, 0.0), axis=1, keepdims=True)
        scale = lax.rsqrt(pivot)
        factor_row = jnp.where(lane >= j, row * scale, 0.0)
        inverse_row = ops_row * scale
        upper_ref[pl.ds(j, 1), :] = factor_row
        inverse_ref[pl.ds(j, 1), :] = inverse_row
        column = jnp.sum(jnp.where(cols == j, rest, 0.0), axis=1, keepdims=True)
        factor_col = jnp.where(sublane > j, column * scale, 0.0)
        rest_ref[...] = rest - factor_col * factor_row
        ops_ref[...] = ops_ref[...] - factor_col * inverse_row
        return carry

    lax.fori_loop(0, size, step, 0, unroll=2)


def factor(gram):
    size = gram.shape[0]
    vmem = pltpu.VMEM
    return pl.pallas_call(
        factor_kernel,
        out_shape=(
            jax.ShapeDtypeStruct((size, size), jnp.float32),
            jax.ShapeDtypeStruct((size, size), jnp.float32),
        ),
        in_specs=[pl.BlockSpec(memory_space=vmem)],
        out_specs=(pl.BlockSpec(memory_space=vmem), pl.BlockSpec(memory_space=vmem)),
        scratch_shapes=[vmem((size, size), jnp.float32), vmem((size, size), jnp.float32)],
    )(gram)


def pack_symmetric(gram):
    half = gram.shape[0] // 2
    rows = lax.broadcasted_iota(jnp.int32, (half, half), 0)
    cols = lax.broadcasted_iota(jnp.int32, (half, half), 1)
    top, corner, bottom = gram[:half, :half], gram[:half, half:], gram[half:, half:]
    folded = jnp.where(rows <= cols, top, bottom)
    diagonal = jnp.sum(jnp.where(rows == cols, bottom, 0.0), axis=0, keepdims=True)
    tail = jnp.concatenate([diagonal, jnp.zeros_like(diagonal)], axis=1)
    return jnp.concatenate([jnp.concatenate([corner, folded], axis=1), tail], axis=0)


def unpack_symmetric(packed):
    half = packed.shape[1] // 2
    rows = lax.broadcasted_iota(jnp.int32, (half, half), 0)
    cols = lax.broadcasted_iota(jnp.int32, (half, half), 1)
    corner, folded = packed[:half, :half], packed[:half, half:]
    diagonal = packed[half : half + 1, :half]
    flipped = folded.T
    top = jnp.where(rows <= cols, folded, flipped)
    bottom = jnp.where(rows > cols, folded, jnp.where(rows < cols, flipped, diagonal))
    upper = jnp.concatenate([top, corner], axis=1)
    lower = jnp.concatenate([corner.T, bottom], axis=1)
    return jnp.concatenate([upper, lower], axis=0)


def tree_sum(values):
    while len(values) > 1:
        values = [values[i] + values[i + 1] for i in range(0, len(values), 2)]
    return values[0]


def gather_sum(value, axes, count):
    stacked = jnp.broadcast_to(value[None], (count,) + value.shape)
    gathered = lax.all_to_all(stacked, axes, 0, 0, tiled=True)
    return tree_sum([gathered[m] for m in range(count)])


def butterfly_sum(value, axis, size):
    bit = 1
    while bit < size:
        pairs = [(i, i ^ bit) for i in range(size)]
        value = value + lax.ppermute(value, axis, pairs)
        bit *= 2
    return value


def along_second(field):
    return (
        8.0 * (jnp.roll(field, -1, 2) - jnp.roll(field, 1, 2))
        - (jnp.roll(field, -2, 2) - jnp.roll(field, 2, 2))
    ) / 12.0


def stencil_rows(padded, row_count):
    return 8.0 * (padded[:, 3 : row_count + 3] - padded[:, 1 : row_count + 1]) - (
        padded[:, 4 : row_count + 4] - padded[:, 0:row_count]
    )


def make_local(sizes):
    total = ring_index(sizes.values())

    def local(velocity):
        snap_count = velocity.shape[1]
        row_count = velocity.shape[2]
        col_count = velocity.shape[3]
        total_cells = row_count * total * col_count
        before, after = halo(velocity, AXES, total, 2)
        comp_u = velocity[0]
        comp_v = velocity[1]
        padded = jnp.concatenate([before, comp_v, after], axis=1)
        u_second = lax.optimization_barrier(along_second(comp_u))
        v_first = stencil_rows(padded, row_count) / 12.0
        vorticity = v_first - u_second
        flattened = vorticity.reshape(snap_count, row_count * col_count)
        local_gram = (
            jnp.dot(
                flattened,
                flattened.T,
                precision=lax.Precision.HIGHEST,
                preferred_element_type=jnp.float32,
            )
            / total_cells
        )
        gram = pack_symmetric(local_gram)
        gram = gather_sum(gram, ("x", "core"), sizes["x"] * sizes["core"])
        gram = gather_sum(gram, ("y",), sizes["y"])
        gram = gather_sum(gram, ("zl",), sizes["zl"])
        gram = gather_sum(gram, ("zh",), sizes["zh"])
        gram = unpack_symmetric(gram)
        upper, inverse_lower = factor(gram)
        spatial_modes = jnp.dot(
            inverse_lower,
            flattened,
            precision=lax.Precision.HIGHEST,
            preferred_element_type=jnp.float32,
        )
        return (spatial_modes.reshape(snap_count, row_count, col_count), upper)

    return local


def solution(mesh):
    devices = mesh.devices.reshape(-1)
    count = devices.shape[0]
    core = 2
    x_size = 4 if count % (core * 4) == 0 else 1
    y_size = 4 if count % (core * x_size * 4) == 0 else 1
    rest = count // (core * x_size * y_size)
    zl = 4 if rest % 4 == 0 else rest
    zh = rest // zl
    sizes = {"zh": zh, "zl": zl, "y": y_size, "x": x_size, "core": core}
    view = Mesh(devices.reshape(zh, zl, y_size, x_size, core), AXES)
    return jax.shard_map(
        make_local(sizes),
        mesh=view,
        in_specs=(P(None, None, AXES, None),),
        out_specs=(P(None, AXES, None), P()),
        check_vma=False,
    )
```

```python
import jax
import jax.numpy as jnp
from jax import lax
from jax.experimental import pallas as pl
from jax.experimental.pallas import tpu as pltpu
from jax.sharding import Mesh
from jax.sharding import PartitionSpec as P

AXES = ("z3", "z21", "z0", "y", "x", "core")


def ring_index(shape):
    size = 1
    for s in shape:
        size *= s
    return size


def extended(array, axes, size, dim, width):
    length = array.shape[dim]
    up = [(i, (i + 1) % size) for i in range(size)]
    down = [(j, i) for i, j in up]
    last = lax.slice_in_dim(array, length - width, length, axis=dim)
    initial = lax.slice_in_dim(array, 0, width, axis=dim)
    before = lax.ppermute(last, axes, up)
    after = lax.ppermute(initial, axes, down)
    return jnp.concatenate([before, array, after], axis=dim)


def factor_kernel(gram_ref, upper_ref, inverse_ref, rest_ref, ops_ref):
    size = gram_ref.shape[0]
    rows = lax.broadcasted_iota(jnp.int32, (size, size), 0)
    cols = lax.broadcasted_iota(jnp.int32, (size, size), 1)
    lane = lax.broadcasted_iota(jnp.int32, (1, size), 1)
    sublane = lax.broadcasted_iota(jnp.int32, (size, 1), 0)
    rest_ref[...] = gram_ref[...]
    ops_ref[...] = jnp.where(rows == cols, 1.0, 0.0).astype(jnp.float32)

    def step(j, carry):
        rest = rest_ref[...]
        row = rest_ref[pl.ds(j, 1), :]
        ops_row = ops_ref[pl.ds(j, 1), :]
        pivot = jnp.sum(jnp.where(lane == j, row, 0.0), axis=1, keepdims=True)
        scale = lax.rsqrt(pivot)
        factor_row = jnp.where(lane >= j, row * scale, 0.0)
        inverse_row = ops_row * scale
        upper_ref[pl.ds(j, 1), :] = factor_row
        inverse_ref[pl.ds(j, 1), :] = inverse_row
        column = jnp.sum(jnp.where(cols == j, rest, 0.0), axis=1, keepdims=True)
        factor_col = jnp.where(sublane > j, column * scale, 0.0)
        rest_ref[...] = rest - factor_col * factor_row
        ops_ref[...] = ops_ref[...] - factor_col * inverse_row
        return carry

    lax.fori_loop(0, size, step, 0, unroll=2)


def factor(gram):
    size = gram.shape[0]
    vmem = pltpu.VMEM
    return pl.pallas_call(
        factor_kernel,
        out_shape=(
            jax.ShapeDtypeStruct((size, size), jnp.float32),
            jax.ShapeDtypeStruct((size, size), jnp.float32),
        ),
        in_specs=[pl.BlockSpec(memory_space=vmem)],
        out_specs=(pl.BlockSpec(memory_space=vmem), pl.BlockSpec(memory_space=vmem)),
        scratch_shapes=[vmem((size, size), jnp.float32), vmem((size, size), jnp.float32)],
    )(gram)


def pack_symmetric(gram):
    half = gram.shape[0] // 2
    rows = lax.broadcasted_iota(jnp.int32, (half, half), 0)
    cols = lax.broadcasted_iota(jnp.int32, (half, half), 1)
    top, corner, bottom = gram[:half, :half], gram[:half, half:], gram[half:, half:]
    folded = jnp.where(rows <= cols, top, bottom)
    diagonal = jnp.sum(jnp.where(rows == cols, bottom, 0.0), axis=0, keepdims=True)
    tail = jnp.concatenate([diagonal, jnp.zeros_like(diagonal)], axis=1)
    return jnp.concatenate([jnp.concatenate([corner, folded], axis=1), tail], axis=0)


def unpack_symmetric(packed):
    half = packed.shape[1] // 2
    rows = lax.broadcasted_iota(jnp.int32, (half, half), 0)
    cols = lax.broadcasted_iota(jnp.int32, (half, half), 1)
    corner, folded = packed[:half, :half], packed[:half, half:]
    diagonal = packed[half : half + 1, :half]
    flipped = folded.T
    top = jnp.where(rows <= cols, folded, flipped)
    bottom = jnp.where(rows > cols, folded, jnp.where(rows < cols, flipped, diagonal))
    upper = jnp.concatenate([top, corner], axis=1)
    lower = jnp.concatenate([corner.T, bottom], axis=1)
    return jnp.concatenate([upper, lower], axis=0)


def tree_sum(values):
    while len(values) > 1:
        values = [values[i] + values[i + 1] for i in range(0, len(values), 2)]
    return values[0]


def gather_sum(value, axes, count):
    stacked = jnp.broadcast_to(value[None], (count,) + value.shape)
    gathered = lax.all_to_all(stacked, axes, 0, 0, tiled=True)
    return tree_sum([gathered[m] for m in range(count)])


def butterfly_sum(value, axis, size):
    bit = 1
    while bit < size:
        pairs = [(i, i ^ bit) for i in range(size)]
        value = value + lax.ppermute(value, axis, pairs)
        bit *= 2
    return value


def along_second(field):
    return (
        8.0 * (jnp.roll(field, -1, 2) - jnp.roll(field, 1, 2))
        - (jnp.roll(field, -2, 2) - jnp.roll(field, 2, 2))
    ) / 12.0


def stencil_rows(padded, row_count):
    return 8.0 * (padded[:, 3 : row_count + 3] - padded[:, 1 : row_count + 1]) - (
        padded[:, 4 : row_count + 4] - padded[:, 0:row_count]
    )


def make_local(sizes):
    total = ring_index(sizes.values())

    def local(velocity):
        snap_count = velocity.shape[1]
        row_count = velocity.shape[2]
        col_count = velocity.shape[3]
        total_cells = row_count * total * col_count
        comp_u = velocity[0]
        comp_v = velocity[1]
        padded = extended(comp_v, AXES, total, 1, 2)
        u_second = lax.optimization_barrier(along_second(comp_u))
        v_first = stencil_rows(padded, row_count) / 12.0
        vorticity = v_first - u_second
        flattened = vorticity.reshape(snap_count, row_count * col_count)
        local_gram = (
            jnp.dot(
                flattened,
                flattened.T,
                precision=lax.Precision.HIGHEST,
                preferred_element_type=jnp.float32,
            )
            / total_cells
        )
        gram = pack_symmetric(local_gram)
        gram = gather_sum(gram, ("x", "core"), sizes["x"] * sizes["core"])
        gram = gather_sum(gram, ("z0", "y"), sizes["z0"] * sizes["y"])
        gram = gather_sum(gram, ("z21",), sizes["z21"])
        gram = gather_sum(gram, ("z3",), sizes["z3"])
        gram = unpack_symmetric(gram)
        upper, inverse_lower = factor(gram)
        spatial_modes = jnp.dot(
            inverse_lower,
            flattened,
            precision=lax.Precision.HIGHEST,
            preferred_element_type=jnp.float32,
        )
        return (spatial_modes.reshape(snap_count, row_count, col_count), upper)

    return local


def solution(mesh):
    devices = mesh.devices.reshape(-1)
    count = devices.shape[0]
    core = 2
    x_size = 4 if count % (core * 4) == 0 else 1
    y_size = 4 if count % (core * x_size * 4) == 0 else 1
    rest = count // (core * x_size * y_size)
    z0 = 2 if rest % 2 == 0 else 1
    z21 = 4 if rest % (z0 * 4) == 0 else 1
    z3 = rest // (z0 * z21)
    sizes = {"z3": z3, "z21": z21, "z0": z0, "y": y_size, "x": x_size, "core": core}
    view = Mesh(devices.reshape(z3, z21, z0, y_size, x_size, core), AXES)
    return jax.shard_map(
        make_local(sizes),
        mesh=view,
        in_specs=(P(None, None, AXES, None),),
        out_specs=(P(None, AXES, None), P()),
        check_vma=False,
    )
```

```python
import jax
import jax.numpy as jnp
from jax import lax
from jax.experimental import pallas as pl
from jax.experimental.pallas import tpu as pltpu
from jax.sharding import Mesh
from jax.sharding import PartitionSpec as P

AXES = ("zh", "zl", "y", "x", "core")


def ring_index(shape):
    size = 1
    for s in shape:
        size *= s
    return size


def extended(array, axes, size, dim, width):
    length = array.shape[dim]
    up = [(i, (i + 1) % size) for i in range(size)]
    down = [(j, i) for i, j in up]
    last = lax.slice_in_dim(array, length - width, length, axis=dim)
    initial = lax.slice_in_dim(array, 0, width, axis=dim)
    before = lax.ppermute(last, axes, up)
    after = lax.ppermute(initial, axes, down)
    return jnp.concatenate([before, array, after], axis=dim)


def factor_kernel(gram_ref, upper_ref, inverse_ref, rest_ref, ops_ref):
    size = gram_ref.shape[0]
    rows = lax.broadcasted_iota(jnp.int32, (size, size), 0)
    cols = lax.broadcasted_iota(jnp.int32, (size, size), 1)
    lane = lax.broadcasted_iota(jnp.int32, (1, size), 1)
    sublane = lax.broadcasted_iota(jnp.int32, (size, 1), 0)
    rest_ref[...] = gram_ref[...]
    ops_ref[...] = jnp.where(rows == cols, 1.0, 0.0).astype(jnp.float32)

    def step(j, carry):
        rest = rest_ref[...]
        row = rest_ref[pl.ds(j, 1), :]
        ops_row = ops_ref[pl.ds(j, 1), :]
        pivot = jnp.sum(jnp.where(lane == j, row, 0.0), axis=1, keepdims=True)
        scale = lax.rsqrt(pivot)
        factor_row = jnp.where(lane >= j, row * scale, 0.0)
        inverse_row = ops_row * scale
        upper_ref[pl.ds(j, 1), :] = factor_row
        inverse_ref[pl.ds(j, 1), :] = inverse_row
        column = jnp.sum(jnp.where(cols == j, rest, 0.0), axis=1, keepdims=True)
        factor_col = jnp.where(sublane > j, column * scale, 0.0)
        rest_ref[...] = rest - factor_col * factor_row
        ops_ref[...] = ops_ref[...] - factor_col * inverse_row
        return carry

    lax.fori_loop(0, size, step, 0, unroll=2)


def factor(gram):
    size = gram.shape[0]
    vmem = pltpu.VMEM
    return pl.pallas_call(
        factor_kernel,
        out_shape=(
            jax.ShapeDtypeStruct((size, size), jnp.float32),
            jax.ShapeDtypeStruct((size, size), jnp.float32),
        ),
        in_specs=[pl.BlockSpec(memory_space=vmem)],
        out_specs=(pl.BlockSpec(memory_space=vmem), pl.BlockSpec(memory_space=vmem)),
        scratch_shapes=[vmem((size, size), jnp.float32), vmem((size, size), jnp.float32)],
    )(gram)


def pack_symmetric(gram):
    half = gram.shape[0] // 2
    rows = lax.broadcasted_iota(jnp.int32, (half, half), 0)
    cols = lax.broadcasted_iota(jnp.int32, (half, half), 1)
    top, corner, bottom = gram[:half, :half], gram[:half, half:], gram[half:, half:]
    folded = jnp.where(rows <= cols, top, bottom)
    diagonal = jnp.sum(jnp.where(rows == cols, bottom, 0.0), axis=0, keepdims=True)
    tail = jnp.concatenate([diagonal, jnp.zeros_like(diagonal)], axis=1)
    return jnp.concatenate([jnp.concatenate([corner, folded], axis=1), tail], axis=0)


def unpack_symmetric(packed):
    half = packed.shape[1] // 2
    rows = lax.broadcasted_iota(jnp.int32, (half, half), 0)
    cols = lax.broadcasted_iota(jnp.int32, (half, half), 1)
    corner, folded = packed[:half, :half], packed[:half, half:]
    diagonal = packed[half : half + 1, :half]
    flipped = folded.T
    top = jnp.where(rows <= cols, folded, flipped)
    bottom = jnp.where(rows > cols, folded, jnp.where(rows < cols, flipped, diagonal))
    upper = jnp.concatenate([top, corner], axis=1)
    lower = jnp.concatenate([corner.T, bottom], axis=1)
    return jnp.concatenate([upper, lower], axis=0)


def tree_sum(values):
    while len(values) > 1:
        values = [values[i] + values[i + 1] for i in range(0, len(values), 2)]
    return values[0]


def gather_sum(value, axes, count):
    stacked = jnp.broadcast_to(value[None], (count,) + value.shape)
    gathered = lax.all_to_all(stacked, axes, 0, 0, tiled=True)
    return tree_sum([gathered[m] for m in range(count)])


def butterfly_sum(value, axis, size):
    bit = 1
    while bit < size:
        pairs = [(i, i ^ bit) for i in range(size)]
        value = value + lax.ppermute(value, axis, pairs)
        bit *= 2
    return value


def along_second(field):
    return (
        8.0 * (jnp.roll(field, -1, 2) - jnp.roll(field, 1, 2))
        - (jnp.roll(field, -2, 2) - jnp.roll(field, 2, 2))
    ) / 12.0


def stencil_rows(padded, row_count):
    return 8.0 * (padded[:, 3 : row_count + 3] - padded[:, 1 : row_count + 1]) - (
        padded[:, 4 : row_count + 4] - padded[:, 0:row_count]
    )


def make_local(sizes):
    total = ring_index(sizes.values())

    def local(velocity):
        snap_count = velocity.shape[1]
        row_count = velocity.shape[2]
        col_count = velocity.shape[3]
        total_cells = row_count * total * col_count
        comp_u = velocity[0]
        comp_v = velocity[1]
        padded = extended(comp_v, AXES, total, 1, 2)
        u_second = lax.optimization_barrier(along_second(comp_u))
        v_first = stencil_rows(padded, row_count) / 12.0
        vorticity = v_first - u_second
        flattened = vorticity.reshape(snap_count, row_count * col_count)
        local_gram = (
            jnp.dot(
                flattened,
                flattened.T,
                precision=lax.Precision.HIGHEST,
                preferred_element_type=jnp.float32,
            )
            / total_cells
        )
        gram = pack_symmetric(local_gram)
        gram = gather_sum(gram, ("zh",), sizes["zh"])
        gram = gather_sum(gram, ("zl",), sizes["zl"])
        gram = gather_sum(gram, ("y",), sizes["y"])
        gram = gather_sum(gram, ("x", "core"), sizes["x"] * sizes["core"])
        gram = unpack_symmetric(gram)
        upper, inverse_lower = factor(gram)
        spatial_modes = jnp.dot(
            inverse_lower,
            flattened,
            precision=lax.Precision.HIGHEST,
            preferred_element_type=jnp.float32,
        )
        return (spatial_modes.reshape(snap_count, row_count, col_count), upper)

    return local


def solution(mesh):
    devices = mesh.devices.reshape(-1)
    count = devices.shape[0]
    core = 2
    x_size = 4 if count % (core * 4) == 0 else 1
    y_size = 4 if count % (core * x_size * 4) == 0 else 1
    rest = count // (core * x_size * y_size)
    zl = 4 if rest % 4 == 0 else rest
    zh = rest // zl
    sizes = {"zh": zh, "zl": zl, "y": y_size, "x": x_size, "core": core}
    view = Mesh(devices.reshape(zh, zl, y_size, x_size, core), AXES)
    return jax.shard_map(
        make_local(sizes),
        mesh=view,
        in_specs=(P(None, None, AXES, None),),
        out_specs=(P(None, AXES, None), P()),
        check_vma=False,
    )
```

```python
import jax
import jax.numpy as jnp
from jax import lax
from jax.experimental import pallas as pl
from jax.experimental.pallas import tpu as pltpu
from jax.sharding import Mesh
from jax.sharding import PartitionSpec as P

AXES = ("zh", "zl", "y", "x", "core")


def ring_index(shape):
    size = 1
    for s in shape:
        size *= s
    return size


def extended(array, axes, size, dim, width):
    length = array.shape[dim]
    up = [(i, (i + 1) % size) for i in range(size)]
    down = [(j, i) for i, j in up]
    last = lax.slice_in_dim(array, length - width, length, axis=dim)
    initial = lax.slice_in_dim(array, 0, width, axis=dim)
    before = lax.ppermute(last, axes, up)
    after = lax.ppermute(initial, axes, down)
    return jnp.concatenate([before, array, after], axis=dim)


def factor_kernel(gram_ref, upper_ref, inverse_ref, rest_ref, ops_ref):
    size = gram_ref.shape[0]
    rows = lax.broadcasted_iota(jnp.int32, (size, size), 0)
    cols = lax.broadcasted_iota(jnp.int32, (size, size), 1)
    lane = lax.broadcasted_iota(jnp.int32, (1, size), 1)
    sublane = lax.broadcasted_iota(jnp.int32, (size, 1), 0)
    rest_ref[...] = gram_ref[...]
    ops_ref[...] = jnp.where(rows == cols, 1.0, 0.0).astype(jnp.float32)

    def step(j, carry):
        rest = rest_ref[...]
        row = rest_ref[pl.ds(j, 1), :]
        ops_row = ops_ref[pl.ds(j, 1), :]
        pivot = jnp.sum(jnp.where(lane == j, row, 0.0), axis=1, keepdims=True)
        scale = lax.rsqrt(pivot)
        factor_row = jnp.where(lane >= j, row * scale, 0.0)
        inverse_row = ops_row * scale
        upper_ref[pl.ds(j, 1), :] = factor_row
        inverse_ref[pl.ds(j, 1), :] = inverse_row
        column = jnp.sum(jnp.where(cols == j, rest, 0.0), axis=1, keepdims=True)
        factor_col = jnp.where(sublane > j, column * scale, 0.0)
        rest_ref[...] = rest - factor_col * factor_row
        ops_ref[...] = ops_ref[...] - factor_col * inverse_row
        return carry

    lax.fori_loop(0, size, step, 0, unroll=2)


def factor(gram):
    size = gram.shape[0]
    vmem = pltpu.VMEM
    return pl.pallas_call(
        factor_kernel,
        out_shape=(
            jax.ShapeDtypeStruct((size, size), jnp.float32),
            jax.ShapeDtypeStruct((size, size), jnp.float32),
        ),
        in_specs=[pl.BlockSpec(memory_space=vmem)],
        out_specs=(pl.BlockSpec(memory_space=vmem), pl.BlockSpec(memory_space=vmem)),
        scratch_shapes=[vmem((size, size), jnp.float32), vmem((size, size), jnp.float32)],
    )(gram)


def pack_symmetric(gram):
    half = gram.shape[0] // 2
    rows = lax.broadcasted_iota(jnp.int32, (half, half), 0)
    cols = lax.broadcasted_iota(jnp.int32, (half, half), 1)
    top, corner, bottom = gram[:half, :half], gram[:half, half:], gram[half:, half:]
    folded = jnp.where(rows <= cols, top, bottom)
    diagonal = jnp.sum(jnp.where(rows == cols, bottom, 0.0), axis=0, keepdims=True)
    tail = jnp.concatenate([diagonal, jnp.zeros_like(diagonal)], axis=1)
    return jnp.concatenate([jnp.concatenate([corner, folded], axis=1), tail], axis=0)


def unpack_symmetric(packed):
    half = packed.shape[1] // 2
    rows = lax.broadcasted_iota(jnp.int32, (half, half), 0)
    cols = lax.broadcasted_iota(jnp.int32, (half, half), 1)
    corner, folded = packed[:half, :half], packed[:half, half:]
    diagonal = packed[half : half + 1, :half]
    flipped = folded.T
    top = jnp.where(rows <= cols, folded, flipped)
    bottom = jnp.where(rows > cols, folded, jnp.where(rows < cols, flipped, diagonal))
    upper = jnp.concatenate([top, corner], axis=1)
    lower = jnp.concatenate([corner.T, bottom], axis=1)
    return jnp.concatenate([upper, lower], axis=0)


def tree_sum(values):
    while len(values) > 1:
        values = [values[i] + values[i + 1] for i in range(0, len(values), 2)]
    return values[0]


def gather_sum(value, axes, count):
    stacked = jnp.broadcast_to(value[None], (count,) + value.shape)
    gathered = lax.all_to_all(stacked, axes, 0, 0, tiled=True)
    return tree_sum([gathered[m] for m in range(count)])


def butterfly_sum(value, axis, size):
    bit = 1
    while bit < size:
        pairs = [(i, i ^ bit) for i in range(size)]
        value = value + lax.ppermute(value, axis, pairs)
        bit *= 2
    return value


def along_second(field):
    return (
        8.0 * (jnp.roll(field, -1, 2) - jnp.roll(field, 1, 2))
        - (jnp.roll(field, -2, 2) - jnp.roll(field, 2, 2))
    ) / 12.0


def stencil_rows(padded, row_count):
    return 8.0 * (padded[:, 3 : row_count + 3] - padded[:, 1 : row_count + 1]) - (
        padded[:, 4 : row_count + 4] - padded[:, 0:row_count]
    )


def make_local(sizes):
    total = ring_index(sizes.values())

    def local(velocity):
        snap_count = velocity.shape[1]
        row_count = velocity.shape[2]
        col_count = velocity.shape[3]
        total_cells = row_count * total * col_count
        comp_u = velocity[0]
        comp_v = velocity[1]
        padded = extended(comp_v, AXES, total, 1, 2)
        edge = jnp.zeros_like(padded[:, :2])
        inner = jnp.concatenate([edge, comp_v, edge], axis=1)
        outer = jnp.concatenate([padded[:, :2], jnp.zeros_like(comp_v), padded[:, row_count + 2 :]], axis=1)
        local_part = lax.optimization_barrier(stencil_rows(inner, row_count) / 12.0 - along_second(comp_u))
        vorticity = local_part + stencil_rows(outer, row_count) / 12.0
        flattened = vorticity.reshape(snap_count, row_count * col_count)
        local_gram = (
            jnp.dot(
                flattened,
                flattened.T,
                precision=lax.Precision.HIGHEST,
                preferred_element_type=jnp.float32,
            )
            / total_cells
        )
        gram = pack_symmetric(local_gram)
        gram = gather_sum(gram, ("x", "core"), sizes["x"] * sizes["core"])
        gram = gather_sum(gram, ("y",), sizes["y"])
        gram = gather_sum(gram, ("zl",), sizes["zl"])
        gram = gather_sum(gram, ("zh",), sizes["zh"])
        gram = unpack_symmetric(gram)
        upper, inverse_lower = factor(gram)
        spatial_modes = jnp.dot(
            inverse_lower,
            flattened,
            precision=lax.Precision.HIGHEST,
            preferred_element_type=jnp.float32,
        )
        return (spatial_modes.reshape(snap_count, row_count, col_count), upper)

    return local


def solution(mesh):
    devices = mesh.devices.reshape(-1)
    count = devices.shape[0]
    core = 2
    x_size = 4 if count % (core * 4) == 0 else 1
    y_size = 4 if count % (core * x_size * 4) == 0 else 1
    rest = count // (core * x_size * y_size)
    zl = 4 if rest % 4 == 0 else rest
    zh = rest // zl
    sizes = {"zh": zh, "zl": zl, "y": y_size, "x": x_size, "core": core}
    view = Mesh(devices.reshape(zh, zl, y_size, x_size, core), AXES)
    return jax.shard_map(
        make_local(sizes),
        mesh=view,
        in_specs=(P(None, None, AXES, None),),
        out_specs=(P(None, AXES, None), P()),
        check_vma=False,
    )
```

```python
import jax
import jax.numpy as jnp
from jax import lax
from jax.experimental import pallas as pl
from jax.experimental.pallas import tpu as pltpu
from jax.sharding import Mesh
from jax.sharding import PartitionSpec as P

AXES = ("zh", "zl", "y", "x", "core")


def ring_index(shape):
    size = 1
    for s in shape:
        size *= s
    return size


def extended(array, axes, size, dim, width):
    length = array.shape[dim]
    up = [(i, (i + 1) % size) for i in range(size)]
    down = [(j, i) for i, j in up]
    last = lax.slice_in_dim(array, length - width, length, axis=dim)
    initial = lax.slice_in_dim(array, 0, width, axis=dim)
    before = lax.ppermute(last, axes, up)
    after = lax.ppermute(initial, axes, down)
    return jnp.concatenate([before, array, after], axis=dim)


def factor_kernel(gram_ref, upper_ref, inverse_ref, rest_ref, ops_ref):
    size = gram_ref.shape[0]
    rows = lax.broadcasted_iota(jnp.int32, (size, size), 0)
    cols = lax.broadcasted_iota(jnp.int32, (size, size), 1)
    lane = lax.broadcasted_iota(jnp.int32, (1, size), 1)
    sublane = lax.broadcasted_iota(jnp.int32, (size, 1), 0)
    rest_ref[...] = gram_ref[...]
    ops_ref[...] = jnp.where(rows == cols, 1.0, 0.0).astype(jnp.float32)

    def step(j, carry):
        rest = rest_ref[...]
        row = rest_ref[pl.ds(j, 1), :]
        ops_row = ops_ref[pl.ds(j, 1), :]
        pivot = jnp.sum(jnp.where(lane == j, row, 0.0), axis=1, keepdims=True)
        scale = lax.rsqrt(pivot)
        factor_row = jnp.where(lane >= j, row * scale, 0.0)
        inverse_row = ops_row * scale
        upper_ref[pl.ds(j, 1), :] = factor_row
        inverse_ref[pl.ds(j, 1), :] = inverse_row
        column = jnp.sum(jnp.where(cols == j, rest, 0.0), axis=1, keepdims=True)
        factor_col = jnp.where(sublane > j, column * scale, 0.0)
        rest_ref[...] = rest - factor_col * factor_row
        ops_ref[...] = ops_ref[...] - factor_col * inverse_row
        return carry

    lax.fori_loop(0, size, step, 0, unroll=4)


def factor(gram):
    size = gram.shape[0]
    vmem = pltpu.VMEM
    return pl.pallas_call(
        factor_kernel,
        out_shape=(
            jax.ShapeDtypeStruct((size, size), jnp.float32),
            jax.ShapeDtypeStruct((size, size), jnp.float32),
        ),
        in_specs=[pl.BlockSpec(memory_space=vmem)],
        out_specs=(pl.BlockSpec(memory_space=vmem), pl.BlockSpec(memory_space=vmem)),
        scratch_shapes=[vmem((size, size), jnp.float32), vmem((size, size), jnp.float32)],
    )(gram)


def pack_symmetric(gram):
    half = gram.shape[0] // 2
    rows = lax.broadcasted_iota(jnp.int32, (half, half), 0)
    cols = lax.broadcasted_iota(jnp.int32, (half, half), 1)
    top, corner, bottom = gram[:half, :half], gram[:half, half:], gram[half:, half:]
    folded = jnp.where(rows <= cols, top, bottom)
    diagonal = jnp.sum(jnp.where(rows == cols, bottom, 0.0), axis=0, keepdims=True)
    tail = jnp.concatenate([diagonal, jnp.zeros_like(diagonal)], axis=1)
    return jnp.concatenate([jnp.concatenate([corner, folded], axis=1), tail], axis=0)


def unpack_symmetric(packed):
    half = packed.shape[1] // 2
    rows = lax.broadcasted_iota(jnp.int32, (half, half), 0)
    cols = lax.broadcasted_iota(jnp.int32, (half, half), 1)
    corner, folded = packed[:half, :half], packed[:half, half:]
    diagonal = packed[half : half + 1, :half]
    flipped = folded.T
    top = jnp.where(rows <= cols, folded, flipped)
    bottom = jnp.where(rows > cols, folded, jnp.where(rows < cols, flipped, diagonal))
    upper = jnp.concatenate([top, corner], axis=1)
    lower = jnp.concatenate([corner.T, bottom], axis=1)
    return jnp.concatenate([upper, lower], axis=0)


def tree_sum(values):
    while len(values) > 1:
        values = [values[i] + values[i + 1] for i in range(0, len(values), 2)]
    return values[0]


def gather_sum(value, axes, count):
    stacked = jnp.broadcast_to(value[None], (count,) + value.shape)
    gathered = lax.all_to_all(stacked, axes, 0, 0, tiled=True)
    return tree_sum([gathered[m] for m in range(count)])


def butterfly_sum(value, axis, size):
    bit = 1
    while bit < size:
        pairs = [(i, i ^ bit) for i in range(size)]
        value = value + lax.ppermute(value, axis, pairs)
        bit *= 2
    return value


def along_second(field):
    return (
        8.0 * (jnp.roll(field, -1, 2) - jnp.roll(field, 1, 2))
        - (jnp.roll(field, -2, 2) - jnp.roll(field, 2, 2))
    ) / 12.0


def stencil_rows(padded, row_count):
    return 8.0 * (padded[:, 3 : row_count + 3] - padded[:, 1 : row_count + 1]) - (
        padded[:, 4 : row_count + 4] - padded[:, 0:row_count]
    )


def make_local(sizes):
    total = ring_index(sizes.values())

    def local(velocity):
        snap_count = velocity.shape[1]
        row_count = velocity.shape[2]
        col_count = velocity.shape[3]
        total_cells = row_count * total * col_count
        comp_u = velocity[0]
        comp_v = velocity[1]
        padded = extended(comp_v, AXES, total, 1, 2)
        edge = jnp.zeros_like(padded[:, :2])
        inner = jnp.concatenate([edge, comp_v, edge], axis=1)
        outer = jnp.concatenate([padded[:, :2], jnp.zeros_like(comp_v), padded[:, row_count + 2 :]], axis=1)
        local_part = lax.optimization_barrier(stencil_rows(inner, row_count) / 12.0 - along_second(comp_u))
        vorticity = local_part + stencil_rows(outer, row_count) / 12.0
        flattened = vorticity.reshape(snap_count, row_count * col_count)
        local_gram = (
            jnp.dot(
                flattened,
                flattened.T,
                precision=lax.Precision.HIGHEST,
                preferred_element_type=jnp.float32,
            )
            / total_cells
        )
        gram = pack_symmetric(local_gram)
        gram = gather_sum(gram, ("x", "core"), sizes["x"] * sizes["core"])
        gram = gather_sum(gram, ("y",), sizes["y"])
        gram = gather_sum(gram, ("zl",), sizes["zl"])
        gram = gather_sum(gram, ("zh",), sizes["zh"])
        gram = unpack_symmetric(gram)
        upper, inverse_lower = factor(gram)
        spatial_modes = jnp.dot(
            inverse_lower,
            flattened,
            precision=lax.Precision.HIGHEST,
            preferred_element_type=jnp.float32,
        )
        return (spatial_modes.reshape(snap_count, row_count, col_count), upper)

    return local


def solution(mesh):
    devices = mesh.devices.reshape(-1)
    count = devices.shape[0]
    core = 2
    x_size = 4 if count % (core * 4) == 0 else 1
    y_size = 4 if count % (core * x_size * 4) == 0 else 1
    rest = count // (core * x_size * y_size)
    zl = 4 if rest % 4 == 0 else rest
    zh = rest // zl
    sizes = {"zh": zh, "zl": zl, "y": y_size, "x": x_size, "core": core}
    view = Mesh(devices.reshape(zh, zl, y_size, x_size, core), AXES)
    return jax.shard_map(
        make_local(sizes),
        mesh=view,
        in_specs=(P(None, None, AXES, None),),
        out_specs=(P(None, AXES, None), P()),
        check_vma=False,
    )
```
